128 devices in a mesh: dp: 8 (over x, core), eig: 16 (over y, z).
Axes of the slice: x: 4, y: 4, z: 4, core: 2. Of those that a mesh axis runs over, the one named last changes fastest.
Arguments:
- acts: bfloat16 [4096, 8192], P(('dp', 'eig')), may hold values from -6 to 6
- grads: bfloat16 [4096, 8192], P(('dp', 'eig')), may hold values from -6 to 6
- act_basis: bfloat16 [4096, 8192], P('eig'), may hold values from -0.0625 to 0.0625
- grad_basis: bfloat16 [4096, 8192], P('eig'), may hold values from -0.0625 to 0.0625
- eigenvalues: float32 [4096, 4096], P('eig'), may hold values from 0.05 to 20
- query_grads: bfloat16 [32, 256, 4096], P('dp', None, 'eig'), may hold values from -6 to 6
- query_acts: bfloat16 [32, 256, 4096], P('dp'), may hold values from -6 to 6
- cand_local: int32 [8, 16], P('dp'), may hold values from 0 to 7, as said below
- seq_lengths: int32 [8, 8], P('dp'), may hold values from 1 to 128, 512 in all within a row
Outputs:
- scores: float32 [32, 16], P('dp')
The draws below stay inside these ranges and needn't reach their ends.
Inputs may be any that keep to these rules, and one draw needn't show every extreme that they name: `cand_local`: entry j of an owner's list names a sequence of dp shard j // 2; the 2 entries of one list that name one shard differ. `seq_lengths`: row d lists the lengths of the 8 sequences packed in order in dp shard d's 512 token rows; they sum to 512.
All inputs are finite; a program needn't handle non-finite values.
Results may differ from the reference program's by a relative error of at most 0.006.
Values may be sent and summed in bfloat16 or wider, within the bound.
No kernel may reach another device: no remote copies, remote signals or barrier semaphores. Data moves between devices by JAX's collectives and lax.ppermute only.
A program may use at most 128 MiB of HBM per device.

```python
import math
import jax
import jax.numpy as jnp
import numpy as np
from jax import lax

D = 8192
KW = 4096
TOK_DEV = 32
SEQ_DP = 8
CAP = 2
QPD = 4
QLEN = 256
TOK_DP = 512
MAXLEN = 128
TOKENS = 4096
CL = 16
NQ = 32
N_DP = 8
N_EIG = 16


def draw_cand_local(key, part):
    owners = CL // CAP
    weights = jax.random.randint(jax.random.fold_in(key, 11), (1, owners, SEQ_DP), 0, 4)
    jitter = jax.random.randint(jax.random.fold_in(key, 12), (owners, owners, SEQ_DP), 0, 1024)
    values = jnp.arange(SEQ_DP, dtype=jnp.int32)[None, None, :]
    owner_ids = jnp.arange(owners, dtype=jnp.int32)[:, None, None]
    forced = (owner_ids == 0) & (values == SEQ_DP - 1) | (owner_ids == 1) & (values == 0)
    scores = (jitter + weights * 400 + forced.astype(jnp.int32) * 8192) * SEQ_DP + values
    top_scores, chosen = lax.top_k(scores, CAP)
    return chosen.reshape(owners, owners * CAP).astype(jnp.int32)


def level_of(own_key, shape, shards, smallest, high):
    factor_of, own = 1.0, jax.random.fold_in(own_key, 6)
    for dim, shards_of in shards:
        draws = jnp.exp(jax.random.uniform(jax.random.fold_in(own, dim), (shards_of,), jnp.float32, smallest / len(shards), high / len(shards)))
        factor_of = factor_of * jnp.repeat(draws, shape[dim] // shards_of).reshape([-1 if axis == dim else 1 for axis in range(len(shape))])
    return factor_of


def length_profile(number_of, total, limit, skew):
    portions = [(1 << 20) // math.isqrt(grade ** skew) + 1 for grade in range(2, number_of + 1)]
    rest, given = total - limit - (number_of - 1), [1] * (number_of - 1)
    while rest > 0:
        free = [i for i in range(number_of - 1) if given[i] < limit]
        whole, left = sum([portions[i] for i in free]), rest
        for i in free:
            addition = min(limit - given[i], max(1, left * portions[i] // whole), rest)
            given[i] = given[i] + addition
            rest = rest - addition
    return np.array([limit] + given)


def uneven(key, amount, total, limit, lean):
    if amount == 2:
        one = jax.random.randint(key, (), max(1, total - limit), min(limit, total - 1) + 1)
        return jnp.stack([one, total - one])
    tallies = jnp.asarray(length_profile(amount, total, limit, lean), jnp.int32)
    couples = (amount - 1) // 2
    giver, taker = tallies[1:1 + 2 * couples:2], tallies[2:2 + 2 * couples:2]
    slack = jnp.minimum(giver - 1, limit - taker)
    moved = jax.random.randint(jax.random.fold_in(key, 1), (couples,), 0, 1 << 20) % (slack + 1)
    tallies = tallies.at[1:1 + 2 * couples:2].set(giver - moved).at[2:2 + 2 * couples:2].set(taker + moved)
    return tallies[jax.random.permutation(jax.random.fold_in(key, 2), amount)]


def noise(key, extent, width, bound, pieces=(), kind=jnp.bfloat16):
    gain = level_of(key, extent, pieces, -0.22, 0.18) if pieces else 1.0
    array = jax.random.normal(key, extent, jnp.float32) * width * gain
    return jnp.minimum(jnp.maximum(array, -bound), bound).astype(kind)


def setup_inputs(seed: int = 0) -> dict:
    keys = jax.random.split(jax.random.key(seed), 10)
    return {
        "acts": noise(keys[0], (TOKENS, D), 1.0, 6.0, ((0, 128),)),
        "grads": noise(keys[1], (TOKENS, D), 1.0, 6.0, ((0, 128),)),
        "act_basis": noise(keys[2], (KW, D), D ** -0.5, 0.0625, ((0, 16),)),
        "grad_basis": noise(keys[3], (KW, D), D ** -0.5, 0.0625, ((0, 16),)),
        "eigenvalues": jnp.clip(jnp.exp(math.log(20.0) - 5.9914645 * jax.random.uniform(keys[4], (KW, KW), jnp.float32) ** level_of(keys[4], (KW, KW), ((0, 16),), -0.2, 0.2)), 0.05, 20.0),
        "query_grads": noise(keys[5], (NQ, QLEN, KW), 1.0, 6.0, ((0, 8), (2, 16))),
        "query_acts": noise(keys[6], (NQ, QLEN, KW), 1.0, 6.0, ((0, 8),)),
        "cand_local": draw_cand_local(jax.random.fold_in(keys[9], 71), 0),
        "seq_lengths": jax.vmap(lambda own: uneven(own, SEQ_DP, TOK_DEV * N_EIG, MAXLEN, 2))(jax.random.split(keys[8], N_DP)).reshape((N_DP, SEQ_DP)).astype(jnp.int32),
    }


DAMPING = 0.1

def reference(acts, grads, act_basis, grad_basis, eigenvalues, query_grads, query_acts, cand_local, seq_lengths):
    act_rot = jnp.dot(acts, act_basis.T, preferred_element_type=jnp.float32).astype(jnp.bfloat16)
    grad_rot = jnp.dot(grads, grad_basis.T, preferred_element_type=jnp.float32).astype(jnp.bfloat16)
    offsets = jnp.cumsum(seq_lengths, axis=1) - seq_lengths
    shard_of = jnp.arange(CL, dtype=jnp.int32) // CAP
    shard_table = jnp.broadcast_to(shard_of[None, :], cand_local.shape)
    pick_len = seq_lengths[shard_table, cand_local]
    pick_start = shard_table * TOK_DP + offsets[shard_table, cand_local]
    within = jnp.arange(MAXLEN, dtype=jnp.int32)
    is_live = within[None, None, :] < pick_len[:, :, None]
    row_index = jnp.where(is_live, pick_start[:, :, None] + within[None, None, :], 0).astype(jnp.int32)
    act_rows = jnp.where(is_live[..., None], act_rot[row_index], jnp.zeros((), jnp.bfloat16)).astype(jnp.bfloat16)
    grad_rows = jnp.where(is_live[..., None], grad_rot[row_index], jnp.zeros((), jnp.bfloat16)).astype(jnp.bfloat16)
    damped = eigenvalues + DAMPING
    score_scale = 1.0 / (KW * 4.0 * math.sqrt(QLEN))

    def score_query(index):
        owner = index // QPD
        act_flat = act_rows[owner].reshape(CL * MAXLEN, KW)
        grad_flat = grad_rows[owner].reshape(CL * MAXLEN, KW).astype(jnp.float32)
        query_outer = jnp.dot(query_grads[index].T, query_acts[index], preferred_element_type=jnp.float32)
        precond = (query_outer / damped).astype(jnp.bfloat16)
        projected = jnp.dot(act_flat, precond.T, preferred_element_type=jnp.float32)
        per_token = lax.optimization_barrier(jnp.sum(projected * grad_flat, axis=1))
        return lax.optimization_barrier(jnp.sum(per_token.reshape(CL, MAXLEN), axis=1)) * score_scale
    return lax.map(score_query, jnp.arange(NQ, dtype=jnp.int32))
```

```python
import math

import jax
import jax.numpy as jnp
from jax import lax
from jax.sharding import PartitionSpec as P

DAMPING = 0.1


def shards(
    acts,
    grads,
    act_basis,
    grad_basis,
    eigenvalues,
    query_grads,
    query_acts,
    cand_local,
    seq_lengths,
):
    block_width = act_basis.shape[0]
    queries = query_grads.shape[0]
    full_width = query_acts.shape[2]
    seq_count = seq_lengths.shape[1]
    group_rows = acts.shape[0] * lax.axis_size("eig")
    max_len = 2 * group_rows // seq_count

    pick_lists = lax.all_to_all(cand_local, "dp", split_axis=1, concat_axis=0, tiled=True)
    owners = pick_lists.shape[0]
    per_shard = pick_lists.shape[1]
    lengths = seq_lengths[0]
    offsets = jnp.cumsum(lengths) - lengths
    chosen = (
        pick_lists[:, :, None] == jnp.arange(seq_count, dtype=jnp.int32)[None, None, :]
    ).astype(jnp.int32)
    pick_len = jnp.sum(chosen * lengths[None, None, :], axis=2)
    pick_start = jnp.sum(chosen * offsets[None, None, :], axis=2)
    within = jnp.arange(max_len, dtype=jnp.int32)
    is_live = within[None, None, :] < pick_len[:, :, None]
    row_index = jnp.where(is_live, pick_start[:, :, None] + within[None, None, :], -1).reshape(-1)
    select = (row_index[:, None] == jnp.arange(group_rows, dtype=jnp.int32)[None, :]).astype(
        jnp.bfloat16
    )

    def rotate_and_pack(rows, basis):
        shard_rows = lax.all_gather(rows, "eig", axis=0, tiled=True)
        rotated = jnp.dot(shard_rows, basis.T, preferred_element_type=jnp.float32).astype(
            jnp.bfloat16
        )
        rotated = lax.optimization_barrier(rotated)
        packed = jnp.dot(select, rotated, preferred_element_type=jnp.float32).astype(jnp.bfloat16)
        packed = packed.reshape(owners, per_shard * max_len, block_width)
        return lax.all_to_all(packed, "dp", split_axis=0, concat_axis=0, tiled=True)

    act_narrow = rotate_and_pack(acts, act_basis)
    act_recv = lax.all_gather(act_narrow, "eig", axis=2, tiled=True)
    grad_recv = rotate_and_pack(grads, grad_basis)

    slot_count = owners * per_shard * max_len
    grad_flat = grad_recv.reshape(slot_count, block_width).astype(jnp.float32)
    act_flat = act_recv.reshape(slot_count, full_width)

    damped = eigenvalues + DAMPING
    query_outer = jnp.einsum(
        "qti,qtk->qik", query_grads, query_acts, preferred_element_type=jnp.float32
    )
    precond = (query_outer / damped[None]).astype(jnp.bfloat16)
    precond = lax.optimization_barrier(precond.reshape(queries * block_width, full_width))
    projected = lax.dot_general(
        act_flat, precond, (((1,), (1,)), ((), ())), preferred_element_type=jnp.float32
    )
    projected = lax.optimization_barrier(projected).reshape(slot_count, queries, block_width)
    per_token = jnp.sum(projected * grad_flat[:, None, :], axis=2)
    partial_sums = jnp.sum(per_token.reshape(owners * per_shard, max_len, queries), axis=1).T

    summed = lax.psum(partial_sums, "eig")
    score_scale = 1.0 / (full_width * 4.0 * math.sqrt(query_acts.shape[1]))
    return summed * score_scale


def solution(mesh):
    placed = (
        P(("dp", "eig"), None),
        P(("dp", "eig"), None),
        P("eig", None),
        P("eig", None),
        P("eig", None),
        P("dp", None, "eig"),
        P("dp", None, None),
        P("dp", None),
        P("dp", None),
    )
    return jax.shard_map(
        shards, mesh=mesh, in_specs=placed, out_specs=P("dp", None), check_vma=False
    )
```

```python
import math

import functools

import jax
import jax.numpy as jnp
from jax import lax
from jax.experimental import pallas as pl
from jax.sharding import PartitionSpec as P

DAMPING = 0.1


def _score_body(queries, width, a_ref, p_ref, g_ref, o_ref):
    a = a_ref[...]
    g = g_ref[...].astype(jnp.float32)
    cols = []
    for q in range(queries):
        proj = lax.dot_general(
            a,
            p_ref[q * width : (q + 1) * width, :],
            (((1,), (1,)), ((), ())),
            preferred_element_type=jnp.float32,
        )
        cols.append(jnp.sum(proj * g, axis=1, keepdims=True))
    o_ref[...] = jnp.concatenate(cols, axis=1)


def score_rows(act_flat, precond, grad_flat, queries, tile=256):
    rows, full = act_flat.shape
    width = grad_flat.shape[1]
    return pl.pallas_call(
        functools.partial(_score_body, queries, width),
        grid=(rows // tile,),
        in_specs=[
            pl.BlockSpec((tile, full), lambda i: (i, 0)),
            pl.BlockSpec((queries * width, full), lambda i: (0, 0)),
            pl.BlockSpec((tile, width), lambda i: (i, 0)),
        ],
        out_specs=pl.BlockSpec((tile, queries), lambda i: (i, 0)),
        out_shape=jax.ShapeDtypeStruct((rows, queries), jnp.float32),
        cost_estimate=pl.CostEstimate(
            flops=2 * rows * full * queries * width,
            transcendentals=0,
            bytes_accessed=2 * (rows * full + queries * width * full + rows * width)
            + 4 * rows * queries,
        ),
    )(act_flat, precond, grad_flat)


def shards(
    acts,
    grads,
    act_basis,
    grad_basis,
    eigenvalues,
    query_grads,
    query_acts,
    cand_local,
    seq_lengths,
):
    block_width = act_basis.shape[0]
    queries = query_grads.shape[0]
    full_width = query_acts.shape[2]
    seq_count = seq_lengths.shape[1]
    group_rows = acts.shape[0] * lax.axis_size("eig")
    max_len = 2 * group_rows // seq_count

    pick_lists = lax.all_to_all(cand_local, "dp", split_axis=1, concat_axis=0, tiled=True)
    owners = pick_lists.shape[0]
    per_shard = pick_lists.shape[1]
    lengths = seq_lengths[0]
    offsets = jnp.cumsum(lengths) - lengths
    chosen = (
        pick_lists[:, :, None] == jnp.arange(seq_count, dtype=jnp.int32)[None, None, :]
    ).astype(jnp.int32)
    pick_len = jnp.sum(chosen * lengths[None, None, :], axis=2)
    pick_start = jnp.sum(chosen * offsets[None, None, :], axis=2)
    within = jnp.arange(max_len, dtype=jnp.int32)
    is_live = within[None, None, :] < pick_len[:, :, None]
    row_index = jnp.where(is_live, pick_start[:, :, None] + within[None, None, :], -1).reshape(-1)
    select = (row_index[:, None] == jnp.arange(group_rows, dtype=jnp.int32)[None, :]).astype(
        jnp.bfloat16
    )

    def rotate_and_pack(rows, basis):
        shard_rows = lax.all_gather(rows, "eig", axis=0, tiled=True)
        rotated = jnp.dot(shard_rows, basis.T, preferred_element_type=jnp.float32).astype(
            jnp.bfloat16
        )
        rotated = lax.optimization_barrier(rotated)
        packed = jnp.dot(select, rotated, preferred_element_type=jnp.float32).astype(jnp.bfloat16)
        packed = packed.reshape(owners, per_shard * max_len, block_width)
        return lax.all_to_all(packed, "dp", split_axis=0, concat_axis=0, tiled=True)

    act_narrow = rotate_and_pack(acts, act_basis)
    act_recv = lax.all_gather(act_narrow, "eig", axis=2, tiled=True)
    grad_recv = rotate_and_pack(grads, grad_basis)

    slot_count = owners * per_shard * max_len
    grad_flat = grad_recv.reshape(slot_count, block_width)
    act_flat = act_recv.reshape(slot_count, full_width)

    damped = eigenvalues + DAMPING
    query_outer = jnp.einsum(
        "qti,qtk->qik", query_grads, query_acts, preferred_element_type=jnp.float32
    )
    precond = (query_outer / damped[None]).astype(jnp.bfloat16)
    precond = lax.optimization_barrier(precond.reshape(queries * block_width, full_width))
    per_token = score_rows(act_flat, precond, grad_flat, queries)
    partial_sums = jnp.sum(per_token.reshape(owners * per_shard, max_len, queries), axis=1).T

    summed = partial_sums
    group = lax.axis_size("eig")
    stride = 1
    while stride < group:
        pairs = [(i, i ^ stride) for i in range(group)]
        summed = summed + lax.ppermute(summed, "eig", pairs)
        stride *= 2
    score_scale = 1.0 / (full_width * 4.0 * math.sqrt(query_acts.shape[1]))
    return summed * score_scale


def solution(mesh):
    placed = (
        P(("dp", "eig"), None),
        P(("dp", "eig"), None),
        P("eig", None),
        P("eig", None),
        P("eig", None),
        P("dp", None, "eig"),
        P("dp", None, None),
        P("dp", None),
        P("dp", None),
    )
    return jax.shard_map(
        shards, mesh=mesh, in_specs=placed, out_specs=P("dp", None), check_vma=False
    )
```

```python
import math

import functools

import jax
import jax.numpy as jnp
from jax import lax
from jax.experimental import pallas as pl
from jax.sharding import PartitionSpec as P

DAMPING = 0.1


def _score_body(queries, width, a_ref, p_ref, g_ref, o_ref):
    a = a_ref[...]
    g = g_ref[...].astype(jnp.float32)
    cols = []
    for q in range(queries):
        proj = lax.dot_general(
            a,
            p_ref[q * width : (q + 1) * width, :],
            (((1,), (1,)), ((), ())),
            preferred_element_type=jnp.float32,
        )
        cols.append(jnp.sum(proj * g, axis=1, keepdims=True))
    o_ref[...] = jnp.concatenate(cols, axis=1)


def score_rows(act_flat, precond, grad_flat, queries, tile=256):
    rows, full = act_flat.shape
    width = grad_flat.shape[1]
    return pl.pallas_call(
        functools.partial(_score_body, queries, width),
        grid=(rows // tile,),
        in_specs=[
            pl.BlockSpec((tile, full), lambda i: (i, 0)),
            pl.BlockSpec((queries * width, full), lambda i: (0, 0)),
            pl.BlockSpec((tile, width), lambda i: (i, 0)),
        ],
        out_specs=pl.BlockSpec((tile, queries), lambda i: (i, 0)),
        out_shape=jax.ShapeDtypeStruct((rows, queries), jnp.float32),
        cost_estimate=pl.CostEstimate(
            flops=2 * rows * full * queries * width,
            transcendentals=0,
            bytes_accessed=2 * (rows * full + queries * width * full + rows * width)
            + 4 * rows * queries,
        ),
    )(act_flat, precond, grad_flat)


def _ring_sum(x, size, stride):
    count = lax.axis_size("eig")
    me = lax.axis_index("eig")
    pos = (me // stride) % size
    values = [x]
    for shift in range(1, size):
        pairs = [
            (i, i - ((i // stride) % size) * stride + (((i // stride) % size + shift) % size) * stride)
            for i in range(count)
        ]
        values.append(lax.ppermute(x, "eig", pairs))
    ordered = jnp.take(jnp.stack(values), (pos - jnp.arange(size, dtype=jnp.int32)) % size, axis=0)
    total = ordered[0]
    for k in range(1, size):
        total = total + ordered[k]
    return total


def eig_sum(x):
    count = lax.axis_size("eig")
    inner = 4 if count % 4 == 0 else count
    x = _ring_sum(x, inner, 1)
    if count > inner:
        x = _ring_sum(x, count // inner, inner)
    return x


def shards(
    acts,
    grads,
    act_basis,
    grad_basis,
    eigenvalues,
    query_grads,
    query_acts,
    cand_local,
    seq_lengths,
):
    block_width = act_basis.shape[0]
    queries = query_grads.shape[0]
    full_width = query_acts.shape[2]
    seq_count = seq_lengths.shape[1]
    group_rows = acts.shape[0] * lax.axis_size("eig")
    max_len = 2 * group_rows // seq_count

    pick_lists = lax.all_to_all(cand_local, "dp", split_axis=1, concat_axis=0, tiled=True)
    owners = pick_lists.shape[0]
    per_shard = pick_lists.shape[1]
    lengths = seq_lengths[0]
    offsets = jnp.cumsum(lengths) - lengths
    chosen = (
        pick_lists[:, :, None] == jnp.arange(seq_count, dtype=jnp.int32)[None, None, :]
    ).astype(jnp.int32)
    pick_len = jnp.sum(chosen * lengths[None, None, :], axis=2)
    pick_start = jnp.sum(chosen * offsets[None, None, :], axis=2)
    within = jnp.arange(max_len, dtype=jnp.int32)
    is_live = within[None, None, :] < pick_len[:, :, None]
    row_index = jnp.where(is_live, pick_start[:, :, None] + within[None, None, :], -1).reshape(-1)
    select = (row_index[:, None] == jnp.arange(group_rows, dtype=jnp.int32)[None, :]).astype(
        jnp.bfloat16
    )

    def dp_exchange(packed):
        count = lax.axis_size("dp")
        me = lax.axis_index("dp")
        received = [packed[me]]
        for shift in range(1, count):
            outgoing = lax.dynamic_index_in_dim(packed, (me + shift) % count, 0, keepdims=False)
            pairs = [(i, (i + shift) % count) for i in range(count)]
            received.append(lax.ppermute(outgoing, "dp", pairs))
        return jnp.stack(received)

    def rotate_and_pack(rows, basis):
        rotated = jnp.dot(rows, basis.T, preferred_element_type=jnp.float32).astype(jnp.bfloat16)
        rotated = lax.optimization_barrier(rotated)
        packed = jnp.dot(select, rotated, preferred_element_type=jnp.float32).astype(jnp.bfloat16)
        packed = packed.reshape(owners, per_shard * max_len, block_width)
        return dp_exchange(packed)

    shard_rows = lax.all_gather(jnp.stack([acts, grads]), "eig", axis=1, tiled=True)
    act_narrow = rotate_and_pack(shard_rows[0], act_basis)
    act_recv = lax.all_gather(act_narrow, "eig", axis=2, tiled=True)
    grad_rows, act_narrow = lax.optimization_barrier((shard_rows[1], act_narrow))
    grad_recv = rotate_and_pack(grad_rows, grad_basis)

    slot_count = owners * per_shard * max_len
    grad_flat = grad_recv.reshape(slot_count, block_width)
    act_flat = act_recv.reshape(slot_count, full_width)

    damped = eigenvalues + DAMPING
    query_outer = jnp.einsum(
        "qti,qtk->qik", query_grads, query_acts, preferred_element_type=jnp.float32
    )
    precond = (query_outer / damped[None]).astype(jnp.bfloat16)
    precond = lax.optimization_barrier(precond.reshape(queries * block_width, full_width))
    per_token = score_rows(act_flat, precond, grad_flat, queries)
    slot_sums = jnp.sum(per_token.reshape(owners, per_shard, max_len, queries), axis=2)
    me = lax.axis_index("dp")
    order = (me - jnp.arange(owners, dtype=jnp.int32)) % owners
    partial_sums = jnp.take(slot_sums, order, axis=0).reshape(owners * per_shard, queries).T

    summed = eig_sum(partial_sums)
    score_scale = 1.0 / (full_width * 4.0 * math.sqrt(query_acts.shape[1]))
    return summed * score_scale


def solution(mesh):
    placed = (
        P(("dp", "eig"), None),
        P(("dp", "eig"), None),
        P("eig", None),
        P("eig", None),
        P("eig", None),
        P("dp", None, "eig"),
        P("dp", None, None),
        P("dp", None),
        P("dp", None),
    )
    return jax.shard_map(
        shards, mesh=mesh, in_specs=placed, out_specs=P("dp", None), check_vma=False
    )
```

```python
import math

import functools

import jax
import jax.numpy as jnp
from jax import lax
from jax.experimental import pallas as pl
from jax.sharding import PartitionSpec as P

DAMPING = 0.1


def _score_body(queries, width, a_ref, p_ref, g_ref, o_ref):
    a = a_ref[...]
    g = g_ref[...].astype(jnp.float32)
    cols = []
    for q in range(queries):
        proj = lax.dot_general(
            a,
            p_ref[q * width : (q + 1) * width, :],
            (((1,), (1,)), ((), ())),
            preferred_element_type=jnp.float32,
        )
        cols.append(jnp.sum(proj * g, axis=1, keepdims=True))
    o_ref[...] = jnp.concatenate(cols, axis=1)


def score_rows(act_flat, precond, grad_flat, queries, tile=256):
    rows, full = act_flat.shape
    width = grad_flat.shape[1]
    return pl.pallas_call(
        functools.partial(_score_body, queries, width),
        grid=(rows // tile,),
        in_specs=[
            pl.BlockSpec((tile, full), lambda i: (i, 0)),
            pl.BlockSpec((queries * width, full), lambda i: (0, 0)),
            pl.BlockSpec((tile, width), lambda i: (i, 0)),
        ],
        out_specs=pl.BlockSpec((tile, queries), lambda i: (i, 0)),
        out_shape=jax.ShapeDtypeStruct((rows, queries), jnp.float32),
        cost_estimate=pl.CostEstimate(
            flops=2 * rows * full * queries * width,
            transcendentals=0,
            bytes_accessed=2 * (rows * full + queries * width * full + rows * width)
            + 4 * rows * queries,
        ),
    )(act_flat, precond, grad_flat)


def _ring_sum(x, size, stride):
    count = lax.axis_size("eig")
    me = lax.axis_index("eig")
    pos = (me // stride) % size
    values = [x]
    for shift in range(1, size):
        pairs = [
            (i, i - ((i // stride) % size) * stride + (((i // stride) % size + shift) % size) * stride)
            for i in range(count)
        ]
        values.append(lax.ppermute(x, "eig", pairs))
    ordered = jnp.take(jnp.stack(values), (pos - jnp.arange(size, dtype=jnp.int32)) % size, axis=0)
    total = ordered[0]
    for k in range(1, size):
        total = total + ordered[k]
    return total


def eig_sum(x):
    count = lax.axis_size("eig")
    inner = 4 if count % 4 == 0 else count
    x = _ring_sum(x, inner, 1)
    if count > inner:
        x = _ring_sum(x, count // inner, inner)
    return x


def shards(
    acts,
    grads,
    act_basis,
    grad_basis,
    eigenvalues,
    query_grads,
    query_acts,
    cand_local,
    seq_lengths,
):
    block_width = act_basis.shape[0]
    queries = query_grads.shape[0]
    full_width = query_acts.shape[2]
    seq_count = seq_lengths.shape[1]
    group_rows = acts.shape[0] * lax.axis_size("eig")
    max_len = 2 * group_rows // seq_count

    pick_lists = lax.all_to_all(cand_local, "dp", split_axis=1, concat_axis=0, tiled=True)
    owners = pick_lists.shape[0]
    per_shard = pick_lists.shape[1]
    lengths = seq_lengths[0]
    offsets = jnp.cumsum(lengths) - lengths
    chosen = (
        pick_lists[:, :, None] == jnp.arange(seq_count, dtype=jnp.int32)[None, None, :]
    ).astype(jnp.int32)
    pick_len = jnp.sum(chosen * lengths[None, None, :], axis=2)
    pick_start = jnp.sum(chosen * offsets[None, None, :], axis=2)
    within = jnp.arange(max_len, dtype=jnp.int32)
    is_live = within[None, None, :] < pick_len[:, :, None]
    row_index = jnp.where(is_live, pick_start[:, :, None] + within[None, None, :], -1).reshape(-1)
    select = (row_index[:, None] == jnp.arange(group_rows, dtype=jnp.int32)[None, :]).astype(
        jnp.bfloat16
    )

    dp_count = lax.axis_size("dp")
    dp_me = lax.axis_index("dp")
    inner = 2 if dp_count % 2 == 0 else 1
    outer = dp_count // inner
    x_me = dp_me // inner
    c_me = dp_me % inner

    def dp_exchange(packed):
        rows, width = packed.shape[1], packed.shape[2]
        blocks = packed.reshape(outer, inner, rows, width)
        held = [lax.dynamic_index_in_dim(blocks, c_me, 1, keepdims=False)]
        for t in range(1, inner):
            outgoing = lax.dynamic_index_in_dim(blocks, (c_me - t) % inner, 1, keepdims=False)
            pairs = [
                (i, (i // inner) * inner + (i % inner - t) % inner) for i in range(dp_count)
            ]
            held.append(lax.ppermute(outgoing, "dp", pairs))
        held = jnp.stack(held, axis=1)
        received = [lax.dynamic_index_in_dim(held, x_me, 0, keepdims=False)]
        for shift in range(1, outer):
            outgoing = lax.dynamic_index_in_dim(held, (x_me + shift) % outer, 0, keepdims=False)
            pairs = [
                (i, ((i // inner + shift) % outer) * inner + i % inner) for i in range(dp_count)
            ]
            received.append(lax.ppermute(outgoing, "dp", pairs))
        return jnp.stack(received).reshape(dp_count, rows, width)

    def rotate_and_pack(rows, basis):
        rotated = jnp.dot(rows, basis.T, preferred_element_type=jnp.float32).astype(jnp.bfloat16)
        rotated = lax.optimization_barrier(rotated)
        packed = jnp.dot(select, rotated, preferred_element_type=jnp.float32).astype(jnp.bfloat16)
        packed = packed.reshape(owners, per_shard * max_len, block_width)
        return dp_exchange(packed)

    shard_rows = lax.all_gather(jnp.stack([acts, grads]), "eig", axis=1, tiled=True)
    act_narrow = rotate_and_pack(shard_rows[0], act_basis)
    act_recv = lax.all_gather(act_narrow, "eig", axis=2, tiled=True)
    grad_rows, act_narrow = lax.optimization_barrier((shard_rows[1], act_narrow))
    grad_recv = rotate_and_pack(grad_rows, grad_basis)

    slot_count = owners * per_shard * max_len
    grad_flat = grad_recv.reshape(slot_count, block_width)
    act_flat = act_recv.reshape(slot_count, full_width)

    damped = eigenvalues + DAMPING
    query_outer = jnp.einsum(
        "qti,qtk->qik", query_grads, query_acts, preferred_element_type=jnp.float32
    )
    precond = (query_outer / damped[None]).astype(jnp.bfloat16)
    precond = lax.optimization_barrier(precond.reshape(queries * block_width, full_width))
    per_token = score_rows(act_flat, precond, grad_flat, queries)
    slot_sums = jnp.sum(per_token.reshape(owners, per_shard, max_len, queries), axis=2)
    sources = jnp.arange(owners, dtype=jnp.int32)
    order = ((x_me - sources // inner) % outer) * inner + (sources % inner - c_me) % inner
    partial_sums = jnp.take(slot_sums, order, axis=0).reshape(owners * per_shard, queries).T

    summed = eig_sum(partial_sums)
    score_scale = 1.0 / (full_width * 4.0 * math.sqrt(query_acts.shape[1]))
    return summed * score_scale


def solution(mesh):
    placed = (
        P(("dp", "eig"), None),
        P(("dp", "eig"), None),
        P("eig", None),
        P("eig", None),
        P("eig", None),
        P("dp", None, "eig"),
        P("dp", None, None),
        P("dp", None),
        P("dp", None),
    )
    return jax.shard_map(
        shards, mesh=mesh, in_specs=placed, out_specs=P("dp", None), check_vma=False
    )
```

```python
import math

import functools

import jax
import jax.numpy as jnp
from jax import lax
from jax.experimental import pallas as pl
from jax.experimental.pallas import tpu as pltpu
from jax.sharding import PartitionSpec as P

DAMPING = 0.1


def _score_body(queries, width, a_ref, p_ref, g_ref, o_ref):
    a = a_ref[...]
    g = g_ref[...].astype(jnp.float32)
    cols = []
    for q in range(queries):
        proj = lax.dot_general(
            a,
            p_ref[q * width : (q + 1) * width, :],
            (((1,), (1,)), ((), ())),
            preferred_element_type=jnp.float32,
        )
        cols.append(jnp.sum(proj * g, axis=1, keepdims=True))
    o_ref[...] = jnp.concatenate(cols, axis=1)


def score_rows(act_flat, precond, grad_flat, queries, tile=256):
    rows, full = act_flat.shape
    width = grad_flat.shape[1]
    return pl.pallas_call(
        functools.partial(_score_body, queries, width),
        grid=(rows // tile,),
        in_specs=[
            pl.BlockSpec((tile, full), lambda i: (i, 0)),
            pl.BlockSpec((queries * width, full), lambda i: (0, 0)),
            pl.BlockSpec((tile, width), lambda i: (i, 0)),
        ],
        out_specs=pl.BlockSpec((tile, queries), lambda i: (i, 0)),
        out_shape=jax.ShapeDtypeStruct((rows, queries), jnp.float32),
        cost_estimate=pl.CostEstimate(
            flops=2 * rows * full * queries * width,
            transcendentals=0,
            bytes_accessed=2 * (rows * full + queries * width * full + rows * width)
            + 4 * rows * queries,
        ),
    )(act_flat, precond, grad_flat)


def _ring_sum(x, size, stride):
    count = lax.axis_size("eig")
    me = lax.axis_index("eig")
    pos = (me // stride) % size
    values = [x]
    for shift in range(1, size):
        pairs = [
            (i, i - ((i // stride) % size) * stride + (((i // stride) % size + shift) % size) * stride)
            for i in range(count)
        ]
        values.append(lax.ppermute(x, "eig", pairs))
    ordered = jnp.take(jnp.stack(values), (pos - jnp.arange(size, dtype=jnp.int32)) % size, axis=0)
    total = ordered[0]
    for k in range(1, size):
        total = total + ordered[k]
    return total


def eig_sum(x):
    count = lax.axis_size("eig")
    inner = 4 if count % 4 == 0 else count
    x = _ring_sum(x, inner, 1)
    if count > inner:
        x = _ring_sum(x, count // inner, inner)
    return x


def _rotate_body(chunks, rows_ref, basis_ref, select_ref, o_ref, acc_ref):
    step = pl.program_id(0)

    @pl.when(step == 0)
    def _():
        acc_ref[...] = jnp.zeros_like(acc_ref)

    acc_ref[...] += lax.dot_general(
        rows_ref[0],
        basis_ref[...],
        (((1,), (1,)), ((), ())),
        preferred_element_type=jnp.float32,
    )

    @pl.when(step == chunks - 1)
    def _():
        rotated = acc_ref[...].astype(jnp.bfloat16)
        o_ref[...] = jnp.dot(
            select_ref[...], rotated, preferred_element_type=jnp.float32
        ).astype(o_ref.dtype)


def rotate_pack(stacked, which, basis, select, chunk=1024):
    _, rows, depth = stacked.shape
    width = basis.shape[0]
    slots = select.shape[0]
    chunks = depth // chunk
    return pl.pallas_call(
        functools.partial(_rotate_body, chunks),
        grid=(chunks,),
        in_specs=[
            pl.BlockSpec((1, rows, chunk), lambda k: (which, 0, k)),
            pl.BlockSpec((width, chunk), lambda k: (0, k)),
            pl.BlockSpec((slots, rows), lambda k: (0, 0)),
        ],
        out_specs=pl.BlockSpec((slots, width), lambda k: (0, 0)),
        out_shape=jax.ShapeDtypeStruct((slots, width), jnp.bfloat16),
        scratch_shapes=[pltpu.VMEM((rows, width), jnp.float32)],
        cost_estimate=pl.CostEstimate(
            flops=2 * rows * depth * width + 2 * slots * rows * width,
            transcendentals=0,
            bytes_accessed=2 * (rows * depth + width * depth + slots * rows + slots * width),
        ),
    )(stacked, basis, select)


def shards(
    acts,
    grads,
    act_basis,
    grad_basis,
    eigenvalues,
    query_grads,
    query_acts,
    cand_local,
    seq_lengths,
):
    block_width = act_basis.shape[0]
    queries = query_grads.shape[0]
    full_width = query_acts.shape[2]
    seq_count = seq_lengths.shape[1]
    group_rows = acts.shape[0] * lax.axis_size("eig")
    max_len = 2 * group_rows // seq_count

    pick_lists = lax.all_to_all(cand_local, "dp", split_axis=1, concat_axis=0, tiled=True)
    owners = pick_lists.shape[0]
    per_shard = pick_lists.shape[1]
    lengths = seq_lengths[0]
    offsets = jnp.cumsum(lengths) - lengths
    chosen = (
        pick_lists[:, :, None] == jnp.arange(seq_count, dtype=jnp.int32)[None, None, :]
    ).astype(jnp.int32)
    pick_len = jnp.sum(chosen * lengths[None, None, :], axis=2)
    pick_start = jnp.sum(chosen * offsets[None, None, :], axis=2)
    within = jnp.arange(max_len, dtype=jnp.int32)
    is_live = within[None, None, :] < pick_len[:, :, None]
    row_index = jnp.where(is_live, pick_start[:, :, None] + within[None, None, :], -1).reshape(-1)
    select = (row_index[:, None] == jnp.arange(group_rows, dtype=jnp.int32)[None, :]).astype(
        jnp.bfloat16
    )

    def dp_exchange(packed):
        count = lax.axis_size("dp")
        me = lax.axis_index("dp")
        received = [packed[me]]
        for shift in range(1, count):
            outgoing = lax.dynamic_index_in_dim(packed, (me + shift) % count, 0, keepdims=False)
            pairs = [(i, (i + shift) % count) for i in range(count)]
            received.append(lax.ppermute(outgoing, "dp", pairs))
        return jnp.stack(received)

    def rotate_and_pack(rows, which, basis):
        packed = rotate_pack(rows, which, basis, select)
        packed = packed.reshape(owners, per_shard * max_len, block_width)
        return dp_exchange(packed)

    shard_rows = lax.all_gather(jnp.stack([acts, grads]), "eig", axis=1, tiled=True)
    act_narrow = rotate_and_pack(shard_rows, 0, act_basis)
    act_recv = lax.all_gather(act_narrow, "eig", axis=2, tiled=True)
    grad_rows, act_narrow = lax.optimization_barrier((shard_rows, act_narrow))
    grad_recv = rotate_and_pack(grad_rows, 1, grad_basis)

    slot_count = owners * per_shard * max_len
    grad_flat = grad_recv.reshape(slot_count, block_width)
    act_flat = act_recv.reshape(slot_count, full_width)

    damped = eigenvalues + DAMPING
    query_outer = jnp.einsum(
        "qti,qtk->qik", query_grads, query_acts, preferred_element_type=jnp.float32
    )
    precond = (query_outer / damped[None]).astype(jnp.bfloat16)
    precond = lax.optimization_barrier(precond.reshape(queries * block_width, full_width))
    per_token = score_rows(act_flat, precond, grad_flat, queries)
    slot_sums = jnp.sum(per_token.reshape(owners, per_shard, max_len, queries), axis=2)
    me = lax.axis_index("dp")
    order = (me - jnp.arange(owners, dtype=jnp.int32)) % owners
    partial_sums = jnp.take(slot_sums, order, axis=0).reshape(owners * per_shard, queries).T

    summed = eig_sum(partial_sums)
    score_scale = 1.0 / (full_width * 4.0 * math.sqrt(query_acts.shape[1]))
    return summed * score_scale


def solution(mesh):
    placed = (
        P(("dp", "eig"), None),
        P(("dp", "eig"), None),
        P("eig", None),
        P("eig", None),
        P("eig", None),
        P("dp", None, "eig"),
        P("dp", None, None),
        P("dp", None),
        P("dp", None),
    )
    return jax.shard_map(
        shards, mesh=mesh, in_specs=placed, out_specs=P("dp", None), check_vma=False
    )
```

```python
import math

import functools

import jax
import jax.numpy as jnp
from jax import lax
from jax.experimental import pallas as pl
from jax.sharding import PartitionSpec as P

DAMPING = 0.1


def _score_body(queries, width, a_ref, p_ref, g_ref, o_ref):
    a = jnp.concatenate([a_ref[e] for e in range(a_ref.shape[0])], axis=1)
    g = g_ref[...].astype(jnp.float32)
    cols = []
    for q in range(queries):
        proj = lax.dot_general(
            a,
            p_ref[q * width : (q + 1) * width, :],
            (((1,), (1,)), ((), ())),
            preferred_element_type=jnp.float32,
        )
        cols.append(jnp.sum(proj * g, axis=1, keepdims=True))
    o_ref[...] = jnp.concatenate(cols, axis=1)


def score_rows(act_blocks, precond, grad_flat, queries, tile=256):
    blocks, rows, width = act_blocks.shape
    full = blocks * width
    return pl.pallas_call(
        functools.partial(_score_body, queries, width),
        grid=(rows // tile,),
        in_specs=[
            pl.BlockSpec((blocks, tile, width), lambda i: (0, i, 0)),
            pl.BlockSpec((queries * width, full), lambda i: (0, 0)),
            pl.BlockSpec((tile, width), lambda i: (i, 0)),
        ],
        out_specs=pl.BlockSpec((tile, queries), lambda i: (i, 0)),
        out_shape=jax.ShapeDtypeStruct((rows, queries), jnp.float32),
        cost_estimate=pl.CostEstimate(
            flops=2 * rows * full * queries * width,
            transcendentals=0,
            bytes_accessed=2 * (rows * full + queries * width * full + rows * width)
            + 4 * rows * queries,
        ),
    )(act_blocks, precond, grad_flat)


def _ring_sum(x, size, stride):
    count = lax.axis_size("eig")
    me = lax.axis_index("eig")
    pos = (me // stride) % size
    values = [x]
    for shift in range(1, size):
        pairs = [
            (i, i - ((i // stride) % size) * stride + (((i // stride) % size + shift) % size) * stride)
            for i in range(count)
        ]
        values.append(lax.ppermute(x, "eig", pairs))
    ordered = jnp.take(jnp.stack(values), (pos - jnp.arange(size, dtype=jnp.int32)) % size, axis=0)
    total = ordered[0]
    for k in range(1, size):
        total = total + ordered[k]
    return total


def eig_sum(x):
    count = lax.axis_size("eig")
    inner = 4 if count % 4 == 0 else count
    x = _ring_sum(x, inner, 1)
    if count > inner:
        x = _ring_sum(x, count // inner, inner)
    return x


def shards(
    acts,
    grads,
    act_basis,
    grad_basis,
    eigenvalues,
    query_grads,
    query_acts,
    cand_local,
    seq_lengths,
):
    block_width = act_basis.shape[0]
    queries = query_grads.shape[0]
    full_width = query_acts.shape[2]
    seq_count = seq_lengths.shape[1]
    group_rows = acts.shape[0] * lax.axis_size("eig")
    max_len = 2 * group_rows // seq_count

    pick_lists = lax.all_to_all(cand_local, "dp", split_axis=1, concat_axis=0, tiled=True)
    owners = pick_lists.shape[0]
    per_shard = pick_lists.shape[1]
    lengths = seq_lengths[0]
    offsets = jnp.cumsum(lengths) - lengths
    chosen = (
        pick_lists[:, :, None] == jnp.arange(seq_count, dtype=jnp.int32)[None, None, :]
    ).astype(jnp.int32)
    pick_len = jnp.sum(chosen * lengths[None, None, :], axis=2)
    pick_start = jnp.sum(chosen * offsets[None, None, :], axis=2)
    within = jnp.arange(max_len, dtype=jnp.int32)
    is_live = within[None, None, :] < pick_len[:, :, None]
    row_index = jnp.where(is_live, pick_start[:, :, None] + within[None, None, :], -1).reshape(-1)
    select = (row_index[:, None] == jnp.arange(group_rows, dtype=jnp.int32)[None, :]).astype(
        jnp.bfloat16
    )

    def dp_exchange(packed):
        count = lax.axis_size("dp")
        me = lax.axis_index("dp")
        received = [packed[me]]
        for shift in range(1, count):
            outgoing = lax.dynamic_index_in_dim(packed, (me + shift) % count, 0, keepdims=False)
            pairs = [(i, (i + shift) % count) for i in range(count)]
            received.append(lax.ppermute(outgoing, "dp", pairs))
        return jnp.stack(received)

    def rotate_and_pack(rows, basis):
        rotated = jnp.dot(rows, basis.T, preferred_element_type=jnp.float32).astype(jnp.bfloat16)
        rotated = lax.optimization_barrier(rotated)
        packed = jnp.dot(select, rotated, preferred_element_type=jnp.float32).astype(jnp.bfloat16)
        packed = packed.reshape(owners, per_shard * max_len, block_width)
        return dp_exchange(packed)

    shard_rows = lax.all_gather(jnp.stack([acts, grads]), "eig", axis=1, tiled=True)
    act_narrow = rotate_and_pack(shard_rows[0], act_basis)
    act_recv = lax.all_gather(
        act_narrow.reshape(-1, block_width), "eig", axis=0, tiled=False
    )
    grad_rows, act_narrow = lax.optimization_barrier((shard_rows[1], act_narrow))
    grad_recv = rotate_and_pack(grad_rows, grad_basis)

    slot_count = owners * per_shard * max_len
    grad_flat = grad_recv.reshape(slot_count, block_width)

    damped = eigenvalues + DAMPING
    query_outer = jnp.einsum(
        "qti,qtk->qik", query_grads, query_acts, preferred_element_type=jnp.float32
    )
    precond = (query_outer / damped[None]).astype(jnp.bfloat16)
    precond = lax.optimization_barrier(precond.reshape(queries * block_width, full_width))
    per_token = score_rows(act_recv, precond, grad_flat, queries)
    slot_sums = jnp.sum(per_token.reshape(owners, per_shard, max_len, queries), axis=2)
    me = lax.axis_index("dp")
    order = (me - jnp.arange(owners, dtype=jnp.int32)) % owners
    partial_sums = jnp.take(slot_sums, order, axis=0).reshape(owners * per_shard, queries).T

    summed = eig_sum(partial_sums)
    score_scale = 1.0 / (full_width * 4.0 * math.sqrt(query_acts.shape[1]))
    return summed * score_scale


def solution(mesh):
    placed = (
        P(("dp", "eig"), None),
        P(("dp", "eig"), None),
        P("eig", None),
        P("eig", None),
        P("eig", None),
        P("dp", None, "eig"),
        P("dp", None, None),
        P("dp", None),
        P("dp", None),
    )
    return jax.shard_map(
        shards, mesh=mesh, in_specs=placed, out_specs=P("dp", None), check_vma=False
    )
```

```python
import math

import functools

import jax
import jax.numpy as jnp
from jax import lax
from jax.experimental import pallas as pl
from jax.sharding import PartitionSpec as P

DAMPING = 0.1


def _score_body(queries, width, a_ref, p_ref, g_ref, o_ref):
    a = jnp.concatenate([a_ref[e] for e in range(a_ref.shape[0])], axis=1)
    g = g_ref[...].astype(jnp.float32)
    cols = []
    for q in range(queries):
        proj = lax.dot_general(
            a,
            p_ref[q * width : (q + 1) * width, :],
            (((1,), (1,)), ((), ())),
            preferred_element_type=jnp.float32,
        )
        cols.append(jnp.sum(proj * g, axis=1, keepdims=True))
    o_ref[...] = jnp.concatenate(cols, axis=1)


def score_rows(act_blocks, precond, grad_flat, queries, tile=256):
    blocks, rows, width = act_blocks.shape
    full = blocks * width
    return pl.pallas_call(
        functools.partial(_score_body, queries, width),
        grid=(rows // tile,),
        in_specs=[
            pl.BlockSpec((blocks, tile, width), lambda i: (0, i, 0)),
            pl.BlockSpec((queries * width, full), lambda i: (0, 0)),
            pl.BlockSpec((tile, width), lambda i: (i, 0)),
        ],
        out_specs=pl.BlockSpec((tile, queries), lambda i: (i, 0)),
        out_shape=jax.ShapeDtypeStruct((rows, queries), jnp.float32),
        cost_estimate=pl.CostEstimate(
            flops=2 * rows * full * queries * width,
            transcendentals=0,
            bytes_accessed=2 * (rows * full + queries * width * full + rows * width)
            + 4 * rows * queries,
        ),
    )(act_blocks, precond, grad_flat)


def _ring_sum(x, size, stride):
    count = lax.axis_size("eig")
    me = lax.axis_index("eig")
    pos = (me // stride) % size
    values = [x]
    for shift in range(1, size):
        pairs = [
            (i, i - ((i // stride) % size) * stride + (((i // stride) % size + shift) % size) * stride)
            for i in range(count)
        ]
        values.append(lax.ppermute(x, "eig", pairs))
    ordered = jnp.take(jnp.stack(values), (pos - jnp.arange(size, dtype=jnp.int32)) % size, axis=0)
    total = ordered[0]
    for k in range(1, size):
        total = total + ordered[k]
    return total


def eig_sum(x):
    count = lax.axis_size("eig")
    inner = 4 if count % 4 == 0 else count
    x = _ring_sum(x, inner, 1)
    if count > inner:
        x = _ring_sum(x, count // inner, inner)
    return x


def shards(
    acts,
    grads,
    act_basis,
    grad_basis,
    eigenvalues,
    query_grads,
    query_acts,
    cand_local,
    seq_lengths,
):
    block_width = act_basis.shape[0]
    queries = query_grads.shape[0]
    full_width = query_acts.shape[2]
    seq_count = seq_lengths.shape[1]
    group_rows = acts.shape[0] * lax.axis_size("eig")
    max_len = 2 * group_rows // seq_count

    pick_lists = lax.all_to_all(cand_local, "dp", split_axis=1, concat_axis=0, tiled=True)
    owners = pick_lists.shape[0]
    per_shard = pick_lists.shape[1]
    lengths = seq_lengths[0]
    offsets = jnp.cumsum(lengths) - lengths
    chosen = (
        pick_lists[:, :, None] == jnp.arange(seq_count, dtype=jnp.int32)[None, None, :]
    ).astype(jnp.int32)
    pick_len = jnp.sum(chosen * lengths[None, None, :], axis=2)
    pick_start = jnp.sum(chosen * offsets[None, None, :], axis=2)
    within = jnp.arange(max_len, dtype=jnp.int32)
    is_live = within[None, None, :] < pick_len[:, :, None]
    row_index = jnp.where(is_live, pick_start[:, :, None] + within[None, None, :], -1).reshape(-1)
    select = (row_index[:, None] == jnp.arange(group_rows, dtype=jnp.int32)[None, :]).astype(
        jnp.bfloat16
    )

    def dp_exchange(packed):
        count = lax.axis_size("dp")
        me = lax.axis_index("dp")
        received = [packed[me]]
        for shift in range(1, count):
            outgoing = lax.dynamic_index_in_dim(packed, (me + shift) % count, 0, keepdims=False)
            pairs = [(i, (i + shift) % count) for i in range(count)]
            received.append(lax.ppermute(outgoing, "dp", pairs))
        return jnp.stack(received)

    def rotate_and_pack(rows, basis):
        rotated = jnp.dot(rows, basis.T, preferred_element_type=jnp.float32).astype(jnp.bfloat16)
        rotated = lax.optimization_barrier(rotated)
        packed = jnp.dot(select, rotated, preferred_element_type=jnp.float32).astype(jnp.bfloat16)
        packed = packed.reshape(owners, per_shard * max_len, block_width)
        return dp_exchange(packed)

    depth = acts.shape[1]
    gathered = lax.all_gather(jnp.concatenate([acts, grads], axis=1), "eig", axis=0, tiled=True)
    shard_rows = [gathered[:, :depth], gathered[:, depth:]]
    act_narrow = rotate_and_pack(shard_rows[0], act_basis)
    act_recv = lax.all_gather(
        act_narrow.reshape(-1, block_width), "eig", axis=0, tiled=False
    )
    grad_rows, act_narrow = lax.optimization_barrier((shard_rows[1], act_narrow))
    grad_recv = rotate_and_pack(grad_rows, grad_basis)

    slot_count = owners * per_shard * max_len
    grad_flat = grad_recv.reshape(slot_count, block_width)

    damped = eigenvalues + DAMPING
    query_outer = jnp.einsum(
        "qti,qtk->qik", query_grads, query_acts, preferred_element_type=jnp.float32
    )
    precond = (query_outer / damped[None]).astype(jnp.bfloat16)
    precond = lax.optimization_barrier(precond.reshape(queries * block_width, full_width))
    per_token = score_rows(act_recv, precond, grad_flat, queries)
    slot_sums = jnp.sum(per_token.reshape(owners, per_shard, max_len, queries), axis=2)
    me = lax.axis_index("dp")
    order = (me - jnp.arange(owners, dtype=jnp.int32)) % owners
    partial_sums = jnp.take(slot_sums, order, axis=0).reshape(owners * per_shard, queries).T

    summed = eig_sum(partial_sums)
    score_scale = 1.0 / (full_width * 4.0 * math.sqrt(query_acts.shape[1]))
    return summed * score_scale


def solution(mesh):
    placed = (
        P(("dp", "eig"), None),
        P(("dp", "eig"), None),
        P("eig", None),
        P("eig", None),
        P("eig", None),
        P("dp", None, "eig"),
        P("dp", None, None),
        P("dp", None),
        P("dp", None),
    )
    return jax.shard_map(
        shards, mesh=mesh, in_specs=placed, out_specs=P("dp", None), check_vma=False
    )
```

```python
import math

import functools

import jax
import jax.numpy as jnp
from jax import lax
from jax.experimental import pallas as pl
from jax.sharding import PartitionSpec as P

DAMPING = 0.1


def _score_body(queries, width, a_ref, p_ref, g_ref, o_ref):
    a = jnp.concatenate([a_ref[e] for e in range(a_ref.shape[0])], axis=1)
    g = g_ref[...].astype(jnp.float32)
    cols = []
    for q in range(queries):
        proj = lax.dot_general(
            a,
            p_ref[q * width : (q + 1) * width, :],
            (((1,), (1,)), ((), ())),
            preferred_element_type=jnp.float32,
        )
        cols.append(jnp.sum(proj * g, axis=1, keepdims=True))
    o_ref[...] = jnp.concatenate(cols, axis=1)


def score_rows(act_blocks, precond, grad_flat, queries, tile=512):
    blocks, rows, width = act_blocks.shape
    full = blocks * width
    return pl.pallas_call(
        functools.partial(_score_body, queries, width),
        grid=(rows // tile,),
        in_specs=[
            pl.BlockSpec((blocks, tile, width), lambda i: (0, i, 0)),
            pl.BlockSpec((queries * width, full), lambda i: (0, 0)),
            pl.BlockSpec((tile, width), lambda i: (i, 0)),
        ],
        out_specs=pl.BlockSpec((tile, queries), lambda i: (i, 0)),
        out_shape=jax.ShapeDtypeStruct((rows, queries), jnp.float32),
        cost_estimate=pl.CostEstimate(
            flops=2 * rows * full * queries * width,
            transcendentals=0,
            bytes_accessed=2 * (rows * full + queries * width * full + rows * width)
            + 4 * rows * queries,
        ),
    )(act_blocks, precond, grad_flat)


def _ring_sum(x, size, stride):
    count = lax.axis_size("eig")
    me = lax.axis_index("eig")
    pos = (me // stride) % size
    values = [x]
    for shift in range(1, size):
        pairs = [
            (i, i - ((i // stride) % size) * stride + (((i // stride) % size + shift) % size) * stride)
            for i in range(count)
        ]
        values.append(lax.ppermute(x, "eig", pairs))
    ordered = jnp.take(jnp.stack(values), (pos - jnp.arange(size, dtype=jnp.int32)) % size, axis=0)
    total = ordered[0]
    for k in range(1, size):
        total = total + ordered[k]
    return total


def eig_sum(x):
    count = lax.axis_size("eig")
    inner = 4 if count % 4 == 0 else count
    x = _ring_sum(x, inner, 1)
    if count > inner:
        x = _ring_sum(x, count // inner, inner)
    return x


def shards(
    acts,
    grads,
    act_basis,
    grad_basis,
    eigenvalues,
    query_grads,
    query_acts,
    cand_local,
    seq_lengths,
):
    block_width = act_basis.shape[0]
    queries = query_grads.shape[0]
    full_width = query_acts.shape[2]
    seq_count = seq_lengths.shape[1]
    group_rows = acts.shape[0] * lax.axis_size("eig")
    max_len = 2 * group_rows // seq_count

    pick_lists = lax.all_to_all(cand_local, "dp", split_axis=1, concat_axis=0, tiled=True)
    owners = pick_lists.shape[0]
    per_shard = pick_lists.shape[1]
    lengths = seq_lengths[0]
    offsets = jnp.cumsum(lengths) - lengths
    chosen = (
        pick_lists[:, :, None] == jnp.arange(seq_count, dtype=jnp.int32)[None, None, :]
    ).astype(jnp.int32)
    pick_len = jnp.sum(chosen * lengths[None, None, :], axis=2)
    pick_start = jnp.sum(chosen * offsets[None, None, :], axis=2)
    within = jnp.arange(max_len, dtype=jnp.int32)
    is_live = within[None, None, :] < pick_len[:, :, None]
    row_index = jnp.where(is_live, pick_start[:, :, None] + within[None, None, :], -1).reshape(-1)
    select = (row_index[:, None] == jnp.arange(group_rows, dtype=jnp.int32)[None, :]).astype(
        jnp.bfloat16
    )

    def dp_exchange(packed):
        count = lax.axis_size("dp")
        me = lax.axis_index("dp")
        received = [packed[me]]
        for shift in range(1, count):
            outgoing = lax.dynamic_index_in_dim(packed, (me + shift) % count, 0, keepdims=False)
            pairs = [(i, (i + shift) % count) for i in range(count)]
            received.append(lax.ppermute(outgoing, "dp", pairs))
        return jnp.stack(received)

    def rotate_and_pack(rows, basis):
        rotated = jnp.dot(rows, basis.T, preferred_element_type=jnp.float32).astype(jnp.bfloat16)
        rotated = lax.optimization_barrier(rotated)
        packed = jnp.dot(select, rotated, preferred_element_type=jnp.float32).astype(jnp.bfloat16)
        packed = packed.reshape(owners, per_shard * max_len, block_width)
        return dp_exchange(packed)

    shard_rows = lax.all_gather(jnp.stack([acts, grads]), "eig", axis=1, tiled=True)
    act_narrow = rotate_and_pack(shard_rows[0], act_basis)
    act_recv = lax.all_gather(
        act_narrow.reshape(-1, block_width), "eig", axis=0, tiled=False
    )
    grad_rows, act_narrow = lax.optimization_barrier((shard_rows[1], act_narrow))
    grad_recv = rotate_and_pack(grad_rows, grad_basis)

    slot_count = owners * per_shard * max_len
    grad_flat = grad_recv.reshape(slot_count, block_width)

    damped = eigenvalues + DAMPING
    query_outer = jnp.einsum(
        "qti,qtk->qik", query_grads, query_acts, preferred_element_type=jnp.float32
    )
    precond = (query_outer / damped[None]).astype(jnp.bfloat16)
    precond = lax.optimization_barrier(precond.reshape(queries * block_width, full_width))
    per_token = score_rows(act_recv, precond, grad_flat, queries)
    slot_sums = jnp.sum(per_token.reshape(owners, per_shard, max_len, queries), axis=2)
    me = lax.axis_index("dp")
    order = (me - jnp.arange(owners, dtype=jnp.int32)) % owners
    partial_sums = jnp.take(slot_sums, order, axis=0).reshape(owners * per_shard, queries).T

    summed = eig_sum(partial_sums)
    score_scale = 1.0 / (full_width * 4.0 * math.sqrt(query_acts.shape[1]))
    return summed * score_scale


def solution(mesh):
    placed = (
        P(("dp", "eig"), None),
        P(("dp", "eig"), None),
        P("eig", None),
        P("eig", None),
        P("eig", None),
        P("dp", None, "eig"),
        P("dp", None, None),
        P("dp", None),
        P("dp", None),
    )
    return jax.shard_map(
        shards, mesh=mesh, in_specs=placed, out_specs=P("dp", None), check_vma=False
    )
```

```python
import math

import functools

import jax
import jax.numpy as jnp
from jax import lax
from jax.experimental import pallas as pl
from jax.sharding import PartitionSpec as P

DAMPING = 0.1


def _score_body(queries, width, segment, a_ref, p_ref, g_ref, o_ref):
    a = jnp.concatenate([a_ref[e] for e in range(a_ref.shape[0])], axis=1)
    g = g_ref[...].astype(jnp.float32)
    rows = g.shape[0]
    cols = []
    for q in range(queries):
        proj = lax.dot_general(
            a,
            p_ref[q * width : (q + 1) * width, :],
            (((1,), (1,)), ((), ())),
            preferred_element_type=jnp.float32,
        )
        terms = (proj * g).reshape(rows // segment, segment, width)
        cols.append(jnp.sum(jnp.sum(terms, axis=2), axis=1, keepdims=True))
    o_ref[0] = jnp.concatenate(cols, axis=1)


def score_rows(act_blocks, precond, grad_flat, queries, segment, tile=256):
    blocks, rows, width = act_blocks.shape
    full = blocks * width
    return pl.pallas_call(
        functools.partial(_score_body, queries, width, segment),
        grid=(rows // tile,),
        in_specs=[
            pl.BlockSpec((blocks, tile, width), lambda i: (0, i, 0)),
            pl.BlockSpec((queries * width, full), lambda i: (0, 0)),
            pl.BlockSpec((tile, width), lambda i: (i, 0)),
        ],
        out_specs=pl.BlockSpec((1, tile // segment, queries), lambda i: (i, 0, 0)),
        out_shape=jax.ShapeDtypeStruct((rows // tile, tile // segment, queries), jnp.float32),
        cost_estimate=pl.CostEstimate(
            flops=2 * rows * full * queries * width,
            transcendentals=0,
            bytes_accessed=2 * (rows * full + queries * width * full + rows * width)
            + 4 * rows * queries,
        ),
    )(act_blocks, precond, grad_flat)


def _ring_sum(x, size, stride):
    count = lax.axis_size("eig")
    me = lax.axis_index("eig")
    pos = (me // stride) % size
    values = [x]
    for shift in range(1, size):
        pairs = [
            (i, i - ((i // stride) % size) * stride + (((i // stride) % size + shift) % size) * stride)
            for i in range(count)
        ]
        values.append(lax.ppermute(x, "eig", pairs))
    if size == 4:
        return (values[0] + values[2]) + (values[1] + values[3])
    ordered = jnp.take(jnp.stack(values), (pos - jnp.arange(size, dtype=jnp.int32)) % size, axis=0)
    total = ordered[0]
    for k in range(1, size):
        total = total + ordered[k]
    return total


def eig_sum(x):
    count = lax.axis_size("eig")
    inner = 4 if count % 4 == 0 else count
    x = _ring_sum(x, inner, 1)
    if count > inner:
        x = _ring_sum(x, count // inner, inner)
    return x


def shards(
    acts,
    grads,
    act_basis,
    grad_basis,
    eigenvalues,
    query_grads,
    query_acts,
    cand_local,
    seq_lengths,
):
    block_width = act_basis.shape[0]
    queries = query_grads.shape[0]
    full_width = query_acts.shape[2]
    seq_count = seq_lengths.shape[1]
    group_rows = acts.shape[0] * lax.axis_size("eig")
    max_len = 2 * group_rows // seq_count

    pick_lists = lax.all_to_all(cand_local, "dp", split_axis=1, concat_axis=0, tiled=True)
    owners = pick_lists.shape[0]
    per_shard = pick_lists.shape[1]
    lengths = seq_lengths[0]
    offsets = jnp.cumsum(lengths) - lengths
    chosen = (
        pick_lists[:, :, None] == jnp.arange(seq_count, dtype=jnp.int32)[None, None, :]
    ).astype(jnp.int32)
    pick_len = jnp.sum(chosen * lengths[None, None, :], axis=2)
    pick_start = jnp.sum(chosen * offsets[None, None, :], axis=2)
    within = jnp.arange(max_len, dtype=jnp.int32)
    is_live = within[None, None, :] < pick_len[:, :, None]
    row_index = jnp.where(is_live, pick_start[:, :, None] + within[None, None, :], -1).reshape(-1)
    select = (row_index[:, None] == jnp.arange(group_rows, dtype=jnp.int32)[None, :]).astype(
        jnp.bfloat16
    )

    def dp_exchange(packed):
        count = lax.axis_size("dp")
        me = lax.axis_index("dp")
        received = [packed[me]]
        for shift in range(1, count):
            outgoing = lax.dynamic_index_in_dim(packed, (me + shift) % count, 0, keepdims=False)
            pairs = [(i, (i + shift) % count) for i in range(count)]
            received.append(lax.ppermute(outgoing, "dp", pairs))
        return jnp.stack(received)

    def rotate_and_pack(rows, basis):
        rotated = jnp.dot(rows, basis.T, preferred_element_type=jnp.float32).astype(jnp.bfloat16)
        rotated = lax.optimization_barrier(rotated)
        packed = jnp.dot(select, rotated, preferred_element_type=jnp.float32).astype(jnp.bfloat16)
        packed = packed.reshape(owners, per_shard * max_len, block_width)
        return dp_exchange(packed)

    shard_rows = lax.all_gather(jnp.stack([acts, grads]), "eig", axis=1, tiled=True)
    act_narrow = rotate_and_pack(shard_rows[0], act_basis)
    act_recv = lax.all_gather(
        act_narrow.reshape(-1, block_width), "eig", axis=0, tiled=False
    )
    grad_rows, act_narrow = lax.optimization_barrier((shard_rows[1], act_narrow))
    grad_recv = rotate_and_pack(grad_rows, grad_basis)

    slot_count = owners * per_shard * max_len
    grad_flat = grad_recv.reshape(slot_count, block_width)

    damped = eigenvalues + DAMPING
    query_outer = jnp.einsum(
        "qti,qtk->qik", query_grads, query_acts, preferred_element_type=jnp.float32
    )
    precond = (query_outer / damped[None]).astype(jnp.bfloat16)
    precond = lax.optimization_barrier(precond.reshape(queries * block_width, full_width))
    slot_sums = score_rows(act_recv, precond, grad_flat, queries, max_len).reshape(
        owners, per_shard, queries
    )
    me = lax.axis_index("dp")
    order = (me - jnp.arange(owners, dtype=jnp.int32)) % owners
    partial_sums = jnp.take(slot_sums, order, axis=0).reshape(owners * per_shard, queries).T

    summed = eig_sum(partial_sums)
    score_scale = 1.0 / (full_width * 4.0 * math.sqrt(query_acts.shape[1]))
    return summed * score_scale


def solution(mesh):
    placed = (
        P(("dp", "eig"), None),
        P(("dp", "eig"), None),
        P("eig", None),
        P("eig", None),
        P("eig", None),
        P("dp", None, "eig"),
        P("dp", None, None),
        P("dp", None),
        P("dp", None),
    )
    return jax.shard_map(
        shards, mesh=mesh, in_specs=placed, out_specs=P("dp", None), check_vma=False
    )
```

```python
import math

import functools

import jax
import jax.numpy as jnp
from jax import lax
from jax.experimental import pallas as pl
from jax.sharding import PartitionSpec as P

DAMPING = 0.1


def _score_body(queries, width, segment, a_ref, p_ref, g_ref, o_ref):
    a = jnp.concatenate([a_ref[e] for e in range(a_ref.shape[0])], axis=1)
    g = g_ref[...].astype(jnp.float32)
    rows = g.shape[0]
    proj_all = lax.dot_general(
        a, p_ref[...], (((1,), (1,)), ((), ())), preferred_element_type=jnp.float32
    )
    cols = []
    for q in range(queries):
        proj = proj_all[:, q * width : (q + 1) * width]
        terms = (proj * g).reshape(rows // segment, segment, width)
        cols.append(jnp.sum(jnp.sum(terms, axis=2), axis=1, keepdims=True))
    o_ref[0] = jnp.concatenate(cols, axis=1)


def score_rows(act_blocks, precond, grad_flat, queries, segment, tile=256):
    blocks, rows, width = act_blocks.shape
    full = blocks * width
    return pl.pallas_call(
        functools.partial(_score_body, queries, width, segment),
        grid=(rows // tile,),
        in_specs=[
            pl.BlockSpec((blocks, tile, width), lambda i: (0, i, 0)),
            pl.BlockSpec((queries * width, full), lambda i: (0, 0)),
            pl.BlockSpec((tile, width), lambda i: (i, 0)),
        ],
        out_specs=pl.BlockSpec((1, tile // segment, queries), lambda i: (i, 0, 0)),
        out_shape=jax.ShapeDtypeStruct((rows // tile, tile // segment, queries), jnp.float32),
        cost_estimate=pl.CostEstimate(
            flops=2 * rows * full * queries * width,
            transcendentals=0,
            bytes_accessed=2 * (rows * full + queries * width * full + rows * width)
            + 4 * rows * queries,
        ),
    )(act_blocks, precond, grad_flat)


def _ring_sum(x, size, stride):
    count = lax.axis_size("eig")
    me = lax.axis_index("eig")
    pos = (me // stride) % size
    values = [x]
    for shift in range(1, size):
        pairs = [
            (i, i - ((i // stride) % size) * stride + (((i // stride) % size + shift) % size) * stride)
            for i in range(count)
        ]
        values.append(lax.ppermute(x, "eig", pairs))
    if size == 4:
        return (values[0] + values[2]) + (values[1] + values[3])
    ordered = jnp.take(jnp.stack(values), (pos - jnp.arange(size, dtype=jnp.int32)) % size, axis=0)
    total = ordered[0]
    for k in range(1, size):
        total = total + ordered[k]
    return total


def eig_sum(x):
    count = lax.axis_size("eig")
    inner = 4 if count % 4 == 0 else count
    x = _ring_sum(x, inner, 1)
    if count > inner:
        x = _ring_sum(x, count // inner, inner)
    return x


def shards(
    acts,
    grads,
    act_basis,
    grad_basis,
    eigenvalues,
    query_grads,
    query_acts,
    cand_local,
    seq_lengths,
):
    block_width = act_basis.shape[0]
    queries = query_grads.shape[0]
    full_width = query_acts.shape[2]
    seq_count = seq_lengths.shape[1]
    group_rows = acts.shape[0] * lax.axis_size("eig")
    max_len = 2 * group_rows // seq_count

    pick_lists = lax.all_to_all(cand_local, "dp", split_axis=1, concat_axis=0, tiled=True)
    owners = pick_lists.shape[0]
    per_shard = pick_lists.shape[1]
    lengths = seq_lengths[0]
    offsets = jnp.cumsum(lengths) - lengths
    chosen = (
        pick_lists[:, :, None] == jnp.arange(seq_count, dtype=jnp.int32)[None, None, :]
    ).astype(jnp.int32)
    pick_len = jnp.sum(chosen * lengths[None, None, :], axis=2)
    pick_start = jnp.sum(chosen * offsets[None, None, :], axis=2)
    within = jnp.arange(max_len, dtype=jnp.int32)
    is_live = within[None, None, :] < pick_len[:, :, None]
    row_index = jnp.where(is_live, pick_start[:, :, None] + within[None, None, :], -1).reshape(-1)
    select = (row_index[:, None] == jnp.arange(group_rows, dtype=jnp.int32)[None, :]).astype(
        jnp.bfloat16
    )

    def dp_exchange(packed):
        count = lax.axis_size("dp")
        me = lax.axis_index("dp")
        received = [packed[me]]
        for shift in range(1, count):
            outgoing = lax.dynamic_index_in_dim(packed, (me + shift) % count, 0, keepdims=False)
            pairs = [(i, (i + shift) % count) for i in range(count)]
            received.append(lax.ppermute(outgoing, "dp", pairs))
        return jnp.stack(received)

    def rotate_and_pack(rows, basis):
        rotated = jnp.dot(rows, basis.T, preferred_element_type=jnp.float32).astype(jnp.bfloat16)
        rotated = lax.optimization_barrier(rotated)
        packed = jnp.dot(select, rotated, preferred_element_type=jnp.float32).astype(jnp.bfloat16)
        packed = packed.reshape(owners, per_shard * max_len, block_width)
        return dp_exchange(packed)

    shard_rows = lax.all_gather(jnp.stack([acts, grads]), "eig", axis=1, tiled=True)
    act_narrow = rotate_and_pack(shard_rows[0], act_basis)
    act_recv = lax.all_gather(
        act_narrow.reshape(-1, block_width), "eig", axis=0, tiled=False
    )
    grad_rows, act_narrow = lax.optimization_barrier((shard_rows[1], act_narrow))
    grad_recv = rotate_and_pack(grad_rows, grad_basis)

    slot_count = owners * per_shard * max_len
    grad_flat = grad_recv.reshape(slot_count, block_width)

    damped = eigenvalues + DAMPING
    query_outer = jnp.einsum(
        "qti,qtk->qik", query_grads, query_acts, preferred_element_type=jnp.float32
    )
    precond = (query_outer / damped[None]).astype(jnp.bfloat16)
    precond = lax.optimization_barrier(precond.reshape(queries * block_width, full_width))
    slot_sums = score_rows(act_recv, precond, grad_flat, queries, max_len).reshape(
        owners, per_shard, queries
    )
    me = lax.axis_index("dp")
    order = (me - jnp.arange(owners, dtype=jnp.int32)) % owners
    partial_sums = jnp.take(slot_sums, order, axis=0).reshape(owners * per_shard, queries).T

    summed = eig_sum(partial_sums)
    score_scale = 1.0 / (full_width * 4.0 * math.sqrt(query_acts.shape[1]))
    return summed * score_scale


def solution(mesh):
    placed = (
        P(("dp", "eig"), None),
        P(("dp", "eig"), None),
        P("eig", None),
        P("eig", None),
        P("eig", None),
        P("dp", None, "eig"),
        P("dp", None, None),
        P("dp", None),
        P("dp", None),
    )
    return jax.shard_map(
        shards, mesh=mesh, in_specs=placed, out_specs=P("dp", None), check_vma=False
    )
```

```python
import math

import functools

import jax
import jax.numpy as jnp
from jax import lax
from jax.experimental import pallas as pl
from jax.sharding import PartitionSpec as P

DAMPING = 0.1


def _score_body(queries, width, segment, a_ref, p_ref, g_ref, o_ref):
    a = jnp.concatenate([a_ref[e] for e in range(a_ref.shape[0])], axis=1)
    g = g_ref[...].astype(jnp.float32)
    rows = g.shape[0]
    proj_all = lax.dot_general(
        a, p_ref[...], (((1,), (1,)), ((), ())), preferred_element_type=jnp.float32
    )
    cols = []
    for q in range(queries):
        proj = proj_all[:, q * width : (q + 1) * width]
        terms = (proj * g).reshape(rows // segment, segment, width)
        cols.append(jnp.sum(jnp.sum(terms, axis=2), axis=1, keepdims=True))
    o_ref[0] = jnp.concatenate(cols, axis=1)


def score_rows(act_blocks, precond, grad_flat, queries, segment, tile=256):
    blocks, rows, width = act_blocks.shape
    full = blocks * width
    return pl.pallas_call(
        functools.partial(_score_body, queries, width, segment),
        grid=(rows // tile,),
        in_specs=[
            pl.BlockSpec((blocks, tile, width), lambda i: (0, i, 0)),
            pl.BlockSpec((queries * width, full), lambda i: (0, 0)),
            pl.BlockSpec((tile, width), lambda i: (i, 0)),
        ],
        out_specs=pl.BlockSpec((1, tile // segment, queries), lambda i: (i, 0, 0)),
        out_shape=jax.ShapeDtypeStruct((rows // tile, tile // segment, queries), jnp.float32),
        cost_estimate=pl.CostEstimate(
            flops=2 * rows * full * queries * width,
            transcendentals=0,
            bytes_accessed=2 * (rows * full + queries * width * full + rows * width)
            + 4 * rows * queries,
        ),
    )(act_blocks, precond, grad_flat)


def _ring_sum(x, size, stride):
    count = lax.axis_size("eig")
    me = lax.axis_index("eig")
    pos = (me // stride) % size
    values = [x]
    for shift in range(1, size):
        pairs = [
            (i, i - ((i // stride) % size) * stride + (((i // stride) % size + shift) % size) * stride)
            for i in range(count)
        ]
        values.append(lax.ppermute(x, "eig", pairs))
    if size == 4:
        return (values[0] + values[2]) + (values[1] + values[3])
    ordered = jnp.take(jnp.stack(values), (pos - jnp.arange(size, dtype=jnp.int32)) % size, axis=0)
    total = ordered[0]
    for k in range(1, size):
        total = total + ordered[k]
    return total


def eig_sum(x):
    count = lax.axis_size("eig")
    inner = 4 if count % 4 == 0 else count
    x = _ring_sum(x, inner, 1)
    if count > inner:
        x = _ring_sum(x, count // inner, inner)
    return x


def shards(
    acts,
    grads,
    act_basis,
    grad_basis,
    eigenvalues,
    query_grads,
    query_acts,
    cand_local,
    seq_lengths,
):
    block_width = act_basis.shape[0]
    queries = query_grads.shape[0]
    full_width = query_acts.shape[2]
    seq_count = seq_lengths.shape[1]
    group_rows = acts.shape[0] * lax.axis_size("eig")
    max_len = 2 * group_rows // seq_count

    pick_lists = lax.all_to_all(cand_local, "dp", split_axis=1, concat_axis=0, tiled=True)
    owners = pick_lists.shape[0]
    per_shard = pick_lists.shape[1]
    lengths = seq_lengths[0]
    offsets = jnp.cumsum(lengths) - lengths
    chosen = (
        pick_lists[:, :, None] == jnp.arange(seq_count, dtype=jnp.int32)[None, None, :]
    ).astype(jnp.int32)
    pick_len = jnp.sum(chosen * lengths[None, None, :], axis=2)
    pick_start = jnp.sum(chosen * offsets[None, None, :], axis=2)
    within = jnp.arange(max_len, dtype=jnp.int32)
    is_live = within[None, None, :] < pick_len[:, :, None]
    row_index = jnp.where(is_live, pick_start[:, :, None] + within[None, None, :], -1).reshape(-1)
    select = (row_index[:, None] == jnp.arange(group_rows, dtype=jnp.int32)[None, :]).astype(
        jnp.bfloat16
    )

    def dp_exchange(packed):
        count = lax.axis_size("dp")
        me = lax.axis_index("dp")
        received = [packed[me]]
        for shift in range(1, count):
            outgoing = lax.dynamic_index_in_dim(packed, (me + shift) % count, 0, keepdims=False)
            pairs = [(i, (i + shift) % count) for i in range(count)]
            received.append(lax.ppermute(outgoing, "dp", pairs))
        return jnp.stack(received)

    def rotate_and_pack(rows, basis):
        rotated = jnp.dot(rows, basis.T, preferred_element_type=jnp.float32).astype(jnp.bfloat16)
        packed = jnp.dot(select, rotated, preferred_element_type=jnp.float32).astype(jnp.bfloat16)
        packed = packed.reshape(owners, per_shard * max_len, block_width)
        return dp_exchange(packed)

    shard_rows = lax.all_gather(jnp.stack([acts, grads]), "eig", axis=1, tiled=True)
    act_narrow = rotate_and_pack(shard_rows[0], act_basis)
    act_recv = lax.all_gather(
        act_narrow.reshape(-1, block_width), "eig", axis=0, tiled=False
    )
    grad_rows, act_narrow = lax.optimization_barrier((shard_rows[1], act_narrow))
    grad_recv = rotate_and_pack(grad_rows, grad_basis)

    slot_count = owners * per_shard * max_len
    grad_flat = grad_recv.reshape(slot_count, block_width)

    damped = eigenvalues + DAMPING
    query_outer = jnp.einsum(
        "qti,qtk->qik", query_grads, query_acts, preferred_element_type=jnp.float32
    )
    precond = (query_outer / damped[None]).astype(jnp.bfloat16)
    precond = lax.optimization_barrier(precond.reshape(queries * block_width, full_width))
    slot_sums = score_rows(act_recv, precond, grad_flat, queries, max_len).reshape(
        owners, per_shard, queries
    )
    summed = eig_sum(slot_sums)
    me = lax.axis_index("dp")
    order = (me - jnp.arange(owners, dtype=jnp.int32)) % owners
    summed = jnp.take(summed, order, axis=0).reshape(owners * per_shard, queries).T
    score_scale = 1.0 / (full_width * 4.0 * math.sqrt(query_acts.shape[1]))
    return summed * score_scale


def solution(mesh):
    placed = (
        P(("dp", "eig"), None),
        P(("dp", "eig"), None),
        P("eig", None),
        P("eig", None),
        P("eig", None),
        P("dp", None, "eig"),
        P("dp", None, None),
        P("dp", None),
        P("dp", None),
    )
    return jax.shard_map(
        shards, mesh=mesh, in_specs=placed, out_specs=P("dp", None), check_vma=False
    )
```

```python
import math

import functools

import jax
import jax.numpy as jnp
from jax import lax
from jax.experimental import pallas as pl
from jax.sharding import PartitionSpec as P

DAMPING = 0.1


def _score_body(queries, width, segment, a_ref, p_ref, g_ref, o_ref):
    a = jnp.concatenate([a_ref[e] for e in range(a_ref.shape[0])], axis=1)
    g = g_ref[...].astype(jnp.float32)
    rows = g.shape[0]
    proj_all = lax.dot_general(
        a, p_ref[...], (((1,), (1,)), ((), ())), preferred_element_type=jnp.float32
    )
    cols = []
    for q in range(queries):
        proj = proj_all[:, q * width : (q + 1) * width]
        terms = (proj * g).reshape(rows // segment, segment, width)
        cols.append(jnp.sum(jnp.sum(terms, axis=2), axis=1, keepdims=True))
    o_ref[0] = jnp.concatenate(cols, axis=1)


def score_rows(act_blocks, precond, grad_flat, queries, segment, tile=256):
    blocks, rows, width = act_blocks.shape
    full = blocks * width
    return pl.pallas_call(
        functools.partial(_score_body, queries, width, segment),
        grid=(rows // tile,),
        in_specs=[
            pl.BlockSpec((blocks, tile, width), lambda i: (0, i, 0)),
            pl.BlockSpec((queries * width, full), lambda i: (0, 0)),
            pl.BlockSpec((tile, width), lambda i: (i, 0)),
        ],
        out_specs=pl.BlockSpec((1, tile // segment, queries), lambda i: (i, 0, 0)),
        out_shape=jax.ShapeDtypeStruct((rows // tile, tile // segment, queries), jnp.float32),
        cost_estimate=pl.CostEstimate(
            flops=2 * rows * full * queries * width,
            transcendentals=0,
            bytes_accessed=2 * (rows * full + queries * width * full + rows * width)
            + 4 * rows * queries,
        ),
    )(act_blocks, precond, grad_flat)


def _ring_sum(x, size, stride):
    count = lax.axis_size("eig")
    me = lax.axis_index("eig")
    pos = (me // stride) % size
    values = [x]
    for shift in range(1, size):
        pairs = [
            (i, i - ((i // stride) % size) * stride + (((i // stride) % size + shift) % size) * stride)
            for i in range(count)
        ]
        values.append(lax.ppermute(x, "eig", pairs))
    if size == 4:
        return (values[0] + values[2]) + (values[1] + values[3])
    ordered = jnp.take(jnp.stack(values), (pos - jnp.arange(size, dtype=jnp.int32)) % size, axis=0)
    total = ordered[0]
    for k in range(1, size):
        total = total + ordered[k]
    return total


def eig_sum(x):
    count = lax.axis_size("eig")
    inner = 4 if count % 4 == 0 else count
    x = _ring_sum(x, inner, 1)
    if count > inner:
        x = _ring_sum(x, count // inner, inner)
    return x


def shards(
    acts,
    grads,
    act_basis,
    grad_basis,
    eigenvalues,
    query_grads,
    query_acts,
    cand_local,
    seq_lengths,
):
    block_width = act_basis.shape[0]
    queries = query_grads.shape[0]
    full_width = query_acts.shape[2]
    seq_count = seq_lengths.shape[1]
    group_rows = acts.shape[0] * lax.axis_size("eig")
    max_len = 2 * group_rows // seq_count

    pick_lists = lax.all_to_all(cand_local, "dp", split_axis=1, concat_axis=0, tiled=True)
    owners = pick_lists.shape[0]
    per_shard = pick_lists.shape[1]
    lengths = seq_lengths[0]
    offsets = jnp.cumsum(lengths) - lengths
    chosen = (
        pick_lists[:, :, None] == jnp.arange(seq_count, dtype=jnp.int32)[None, None, :]
    ).astype(jnp.int32)
    pick_len = jnp.sum(chosen * lengths[None, None, :], axis=2)
    pick_start = jnp.sum(chosen * offsets[None, None, :], axis=2)
    within = jnp.arange(max_len, dtype=jnp.int32)
    is_live = within[None, None, :] < pick_len[:, :, None]
    row_index = jnp.where(is_live, pick_start[:, :, None] + within[None, None, :], -1).reshape(-1)
    select = (row_index[:, None] == jnp.arange(group_rows, dtype=jnp.int32)[None, :]).astype(
        jnp.bfloat16
    )

    def dp_exchange(packed):
        count = lax.axis_size("dp")
        me = lax.axis_index("dp")
        received = [packed[me]]
        for shift in range(1, count):
            outgoing = lax.dynamic_index_in_dim(packed, (me + shift) % count, 0, keepdims=False)
            pairs = [(i, (i + shift) % count) for i in range(count)]
            received.append(lax.ppermute(outgoing, "dp", pairs))
        return jnp.stack(received)

    def rotate_and_pack(rows, basis):
        rotated = jnp.dot(rows, basis.T, preferred_element_type=jnp.float32).astype(jnp.bfloat16)
        rotated = lax.optimization_barrier(rotated)
        packed = jnp.dot(select, rotated, preferred_element_type=jnp.float32).astype(jnp.bfloat16)
        packed = packed.reshape(owners, per_shard * max_len, block_width)
        return dp_exchange(packed)

    shard_rows = lax.all_gather(jnp.stack([acts, grads]), "eig", axis=1, tiled=True)
    act_narrow = rotate_and_pack(shard_rows[0], act_basis)
    act_recv = lax.all_gather(
        act_narrow.reshape(-1, block_width), "eig", axis=0, tiled=False
    )
    grad_rows, act_narrow = lax.optimization_barrier((shard_rows[1], act_narrow))
    grad_recv = rotate_and_pack(grad_rows, grad_basis)

    slot_count = owners * per_shard * max_len
    grad_flat = grad_recv.reshape(slot_count, block_width)

    damped = eigenvalues + DAMPING
    query_outer = jnp.einsum(
        "qti,qtk->qik", query_grads, query_acts, preferred_element_type=jnp.float32
    )
    precond = (query_outer / damped[None]).astype(jnp.bfloat16)
    precond = lax.optimization_barrier(precond.reshape(queries * block_width, full_width))
    slot_sums = score_rows(act_recv, precond, grad_flat, queries, max_len).reshape(
        owners, per_shard, queries
    )
    summed = eig_sum(slot_sums)
    me = lax.axis_index("dp")
    order = (me - jnp.arange(owners, dtype=jnp.int32)) % owners
    summed = jnp.take(summed, order, axis=0).reshape(owners * per_shard, queries).T
    score_scale = 1.0 / (full_width * 4.0 * math.sqrt(query_acts.shape[1]))
    return summed * score_scale


def solution(mesh):
    placed = (
        P(("dp", "eig"), None),
        P(("dp", "eig"), None),
        P("eig", None),
        P("eig", None),
        P("eig", None),
        P("dp", None, "eig"),
        P("dp", None, None),
        P("dp", None),
        P("dp", None),
    )
    return jax.shard_map(
        shards, mesh=mesh, in_specs=placed, out_specs=P("dp", None), check_vma=False
    )
```

```python
import math

import functools

import jax
import jax.numpy as jnp
from jax import lax
from jax.experimental import pallas as pl
from jax.experimental.pallas import tpu as pltpu
from jax.sharding import PartitionSpec as P

DAMPING = 0.1


def _score_body(queries, width, segment, a_ref, p_ref, g_ref, o_ref):
    a = jnp.concatenate([a_ref[e] for e in range(a_ref.shape[0])], axis=1)
    g = g_ref[...].astype(jnp.float32)
    rows = g.shape[0]
    proj_all = lax.dot_general(
        a, p_ref[...], (((1,), (1,)), ((), ())), preferred_element_type=jnp.float32
    )
    cols = []
    for q in range(queries):
        proj = proj_all[:, q * width : (q + 1) * width]
        terms = (proj * g).reshape(rows // segment, segment, width)
        cols.append(jnp.sum(jnp.sum(terms, axis=2), axis=1, keepdims=True))
    o_ref[0] = jnp.concatenate(cols, axis=1)


def score_rows(act_blocks, precond, grad_flat, queries, segment, tile=256):
    blocks, rows, width = act_blocks.shape
    full = blocks * width
    return pl.pallas_call(
        functools.partial(_score_body, queries, width, segment),
        grid=(rows // tile,),
        in_specs=[
            pl.BlockSpec((blocks, tile, width), lambda i: (0, i, 0)),
            pl.BlockSpec((queries * width, full), lambda i: (0, 0)),
            pl.BlockSpec((tile, width), lambda i: (i, 0)),
        ],
        out_specs=pl.BlockSpec((1, tile // segment, queries), lambda i: (i, 0, 0)),
        out_shape=jax.ShapeDtypeStruct((rows // tile, tile // segment, queries), jnp.float32),
        compiler_params=pltpu.CompilerParams(),
        cost_estimate=pl.CostEstimate(
            flops=2 * rows * full * queries * width,
            transcendentals=0,
            bytes_accessed=2 * (rows * full + queries * width * full + rows * width)
            + 4 * rows * queries,
        ),
    )(act_blocks, precond, grad_flat)


def _ring_sum(x, size, stride):
    count = lax.axis_size("eig")
    me = lax.axis_index("eig")
    pos = (me // stride) % size
    values = [x]
    for shift in range(1, size):
        pairs = [
            (i, i - ((i // stride) % size) * stride + (((i // stride) % size + shift) % size) * stride)
            for i in range(count)
        ]
        values.append(lax.ppermute(x, "eig", pairs))
    if size == 4:
        return (values[0] + values[2]) + (values[1] + values[3])
    ordered = jnp.take(jnp.stack(values), (pos - jnp.arange(size, dtype=jnp.int32)) % size, axis=0)
    total = ordered[0]
    for k in range(1, size):
        total = total + ordered[k]
    return total


def eig_sum(x):
    count = lax.axis_size("eig")
    inner = 4 if count % 4 == 0 else count
    x = _ring_sum(x, inner, 1)
    if count > inner:
        x = _ring_sum(x, count // inner, inner)
    return x


def shards(
    acts,
    grads,
    act_basis,
    grad_basis,
    eigenvalues,
    query_grads,
    query_acts,
    cand_local,
    seq_lengths,
):
    block_width = act_basis.shape[0]
    queries = query_grads.shape[0]
    full_width = query_acts.shape[2]
    seq_count = seq_lengths.shape[1]
    group_rows = acts.shape[0] * lax.axis_size("eig")
    max_len = 2 * group_rows // seq_count

    pick_lists = lax.all_to_all(cand_local, "dp", split_axis=1, concat_axis=0, tiled=True)
    owners = pick_lists.shape[0]
    per_shard = pick_lists.shape[1]
    lengths = seq_lengths[0]
    offsets = jnp.cumsum(lengths) - lengths
    chosen = (
        pick_lists[:, :, None] == jnp.arange(seq_count, dtype=jnp.int32)[None, None, :]
    ).astype(jnp.int32)
    pick_len = jnp.sum(chosen * lengths[None, None, :], axis=2)
    pick_start = jnp.sum(chosen * offsets[None, None, :], axis=2)
    within = jnp.arange(max_len, dtype=jnp.int32)
    is_live = within[None, None, :] < pick_len[:, :, None]
    row_index = jnp.where(is_live, pick_start[:, :, None] + within[None, None, :], -1).reshape(-1)
    select = (row_index[:, None] == jnp.arange(group_rows, dtype=jnp.int32)[None, :]).astype(
        jnp.bfloat16
    )

    def dp_exchange(packed):
        count = lax.axis_size("dp")
        me = lax.axis_index("dp")
        received = [packed[me]]
        for shift in range(1, count):
            outgoing = lax.dynamic_index_in_dim(packed, (me + shift) % count, 0, keepdims=False)
            pairs = [(i, (i + shift) % count) for i in range(count)]
            received.append(lax.ppermute(outgoing, "dp", pairs))
        return jnp.stack(received)

    def rotate_and_pack(rows, basis):
        rotated = jnp.dot(rows, basis.T, preferred_element_type=jnp.float32).astype(jnp.bfloat16)
        rotated = lax.optimization_barrier(rotated)
        packed = jnp.dot(select, rotated, preferred_element_type=jnp.float32).astype(jnp.bfloat16)
        packed = packed.reshape(owners, per_shard * max_len, block_width)
        return dp_exchange(packed)

    shard_rows = lax.all_gather(jnp.stack([acts, grads]), "eig", axis=1, tiled=True)
    act_narrow = rotate_and_pack(shard_rows[0], act_basis)
    act_recv = lax.all_gather(
        act_narrow.reshape(-1, block_width), "eig", axis=0, tiled=False
    )
    grad_rows, act_narrow = lax.optimization_barrier((shard_rows[1], act_narrow))
    grad_recv = rotate_and_pack(grad_rows, grad_basis)

    slot_count = owners * per_shard * max_len
    grad_flat = grad_recv.reshape(slot_count, block_width)

    damped = eigenvalues + DAMPING
    query_outer = jnp.einsum(
        "qti,qtk->qik", query_grads, query_acts, preferred_element_type=jnp.float32
    )
    precond = (query_outer / damped[None]).astype(jnp.bfloat16)
    precond = lax.optimization_barrier(precond.reshape(queries * block_width, full_width))
    slot_sums = score_rows(act_recv, precond, grad_flat, queries, max_len).reshape(
        owners, per_shard, queries
    )
    me = lax.axis_index("dp")
    order = (me - jnp.arange(owners, dtype=jnp.int32)) % owners
    partial_sums = jnp.take(slot_sums, order, axis=0).reshape(owners * per_shard, queries).T

    summed = eig_sum(partial_sums)
    score_scale = 1.0 / (full_width * 4.0 * math.sqrt(query_acts.shape[1]))
    return summed * score_scale


def solution(mesh):
    placed = (
        P(("dp", "eig"), None),
        P(("dp", "eig"), None),
        P("eig", None),
        P("eig", None),
        P("eig", None),
        P("dp", None, "eig"),
        P("dp", None, None),
        P("dp", None),
        P("dp", None),
    )
    return jax.shard_map(
        shards, mesh=mesh, in_specs=placed, out_specs=P("dp", None), check_vma=False
    )
```
